32 devices in a mesh: dp: 4 (over y, x), seq: 8 (over z, core).
Axes of the slice: x: 2, y: 2, z: 4, core: 2. Of those that a mesh axis runs over, the one named last changes fastest.
Arguments:
- queries: bfloat16 [6144, 2048], P(('dp', 'seq')), may hold values from -16 to 16
- keys: bfloat16 [6144, 2048], P(('dp', 'seq')), may hold values from -16 to 16
- values: bfloat16 [6144, 2048], P(('dp', 'seq')), may hold values from -6 to 6
- out_grad: bfloat16 [6144, 2048], P(('dp', 'seq')), may hold values from -6 to 6
- out_weight: bfloat16 [2048, 2048], P('dp'), may hold values from -0.125 to 0.125
- section_ids: int32 [6144], P(('dp', 'seq')), may hold values from 0 to 95, as said below
- masked: int32 [6144], P(('dp', 'seq')), may hold values from 0 to 1, as said below
Outputs:
- query_grad: bfloat16 [6144, 2048], P(('dp', 'seq'))
- key_grad: bfloat16 [6144, 2048], P(('dp', 'seq'))
- value_grad: bfloat16 [6144, 2048], P(('dp', 'seq'))
- weight_grad: float32 [2048, 2048], P('dp')
The draws below stay inside these ranges and needn't reach their ends.
Inputs may be any that keep to these rules, and one draw needn't show every extreme that they name: `section_ids`: section numbers never fall along the tokens, are constant over each aligned block of 64 tokens, and no section spans two sequences of 1536 tokens. `masked`: the same for all tokens of a section.
All inputs are finite; a program needn't handle non-finite values.
Results may differ from the reference program's by a relative error of at most 0.015.
Values may be sent and summed in bfloat16 or wider, within the bound.
No kernel may reach another device: no remote copies, remote signals or barrier semaphores. Data moves between devices by JAX's collectives and lax.ppermute only.
A program may use at most 128 MiB of HBM per device.

```python
import jax
import jax.numpy as jnp
from jax import lax

D = 2048
HEADS = 16
HEAD_DIM = 128
BLOCK = 64
SEQ_LEN = 1536
TOKENS = 6144
N_DP = 4


def query_key_pair(key):
    width = HEADS * HEAD_DIM
    base_key = jax.random.fold_in(key, 101)
    key_query, key_keys = jax.random.split(base_key, 2)
    query_vals = jnp.clip(jax.random.normal(key_query, (TOKENS, width), jnp.float32), -4.0, 4.0)
    key_vals = jnp.clip(jax.random.normal(key_keys, (TOKENS, width), jnp.float32), -3.5, 3.5)
    return (query_vals, key_vals)


def draw_queries(key, part):
    return query_key_pair(key)[0].astype(jnp.bfloat16)


def draw_keys(key, part):
    return query_key_pair(key)[1].astype(jnp.bfloat16)


def section_layout(key):
    blocks = TOKENS // BLOCK
    per_seq = SEQ_LEN // BLOCK
    index = jnp.arange(blocks).astype(jnp.int32)
    fresh = jax.random.randint(jax.random.fold_in(key, 211), (blocks,), 0, 3) == 0
    fresh = fresh | (index % per_seq == 0) | (index == blocks - 1)
    starts = jnp.where(fresh, index, 0).astype(jnp.int32)
    ids_blocks = lax.cummax(starts, axis=0).astype(jnp.int32)
    table = jax.random.randint(jax.random.fold_in(key, 223), (blocks,), 0, 2).astype(jnp.int32)
    flag_blocks = table[ids_blocks]
    return (jnp.repeat(ids_blocks, BLOCK, total_repeat_length=TOKENS), jnp.repeat(flag_blocks, BLOCK, total_repeat_length=TOKENS))


def draw_section_ids(key, part):
    return section_layout(key)[0]


def draw_masked(key, part):
    return section_layout(key)[1]


def level_of(own_key, shape, shards, least, top_value):
    def one(axis_at, parts):
        steps = jax.random.uniform(jax.random.fold_in(jax.random.fold_in(own_key, 6), axis_at), (parts,), jnp.float32, least / len(shards), top_value / len(shards))
        return jnp.repeat(jnp.exp(steps), shape[axis_at] // parts).reshape((-1,) + (1,) * (len(shape) - axis_at - 1))

    factor_of = one(*shards[0])
    for cut in shards[1:]:
        factor_of = factor_of * one(*cut)
    return factor_of


def normal_values(key, dims, scale, reach, pieces=(), held_as=jnp.bfloat16):
    result = scale * jax.random.normal(key, dims, jnp.float32)
    if pieces:
        result = result * level_of(key, dims, pieces, -0.22, 0.18)
    return jnp.clip(result, -reach, reach).astype(held_as)


def setup_inputs(seed: int = 0) -> dict:
    streams_of = jax.random.split(jax.random.key(seed), 8)
    return {
        "queries": draw_queries(jax.random.fold_in(streams_of[7], 71), 0),
        "keys": draw_keys(jax.random.fold_in(streams_of[7], 71), 0),
        "values": normal_values(streams_of[2], (TOKENS, HEADS * HEAD_DIM), 1.0, 6.0, ((0, 32),)),
        "out_grad": normal_values(streams_of[3], (TOKENS, D), 1.0, 6.0, ((0, 32),)),
        "out_weight": normal_values(streams_of[4], (HEADS * HEAD_DIM, D), (HEADS * HEAD_DIM) ** -0.5, 0.125, ((0, 4),)),
        "section_ids": draw_section_ids(jax.random.fold_in(streams_of[7], 71), 0),
        "masked": draw_masked(jax.random.fold_in(streams_of[7], 71), 0),
    }


def head_backward(query_h, key_h, value_h, grad_h, sections, flags):
    score_scale = HEAD_DIM ** -0.5
    scores = jnp.dot(query_h, key_h.T, preferred_element_type=jnp.float32) * score_scale
    allowed = (flags[None, :] == 0) | (sections[:, None] == sections[None, :])
    scores = jnp.where(allowed, scores, -1e30)
    row_max = jnp.max(scores, axis=1, keepdims=True)
    exp_scores = jnp.exp(scores - row_max)
    attn_probs = exp_scores / jnp.sum(exp_scores, axis=1, keepdims=True)
    probs_low = attn_probs.astype(jnp.bfloat16)
    attn_out = jnp.dot(probs_low, value_h, preferred_element_type=jnp.float32).astype(jnp.bfloat16)
    row_delta = jnp.sum(grad_h.astype(jnp.float32) * attn_out.astype(jnp.float32), axis=1)
    prob_grad = jnp.dot(grad_h, value_h.T, preferred_element_type=jnp.float32)
    score_grad = (attn_probs * (prob_grad - row_delta[:, None])).astype(jnp.bfloat16)
    query_grad = (jnp.dot(score_grad, key_h, preferred_element_type=jnp.float32) * score_scale).astype(jnp.bfloat16)
    key_grad = (jnp.dot(score_grad.T, query_h, preferred_element_type=jnp.float32) * score_scale).astype(jnp.bfloat16)
    value_grad = jnp.dot(probs_low.T, grad_h, preferred_element_type=jnp.float32).astype(jnp.bfloat16)
    return attn_out, query_grad, key_grad, value_grad


def reference(queries, keys, values, out_grad, out_weight, section_ids, masked):
    width = HEADS * HEAD_DIM
    attn_grad = jnp.dot(out_grad, out_weight.T, preferred_element_type=jnp.float32).astype(jnp.bfloat16)

    def to_heads(array):
        return array.reshape(N_DP, SEQ_LEN, HEADS, HEAD_DIM).transpose(0, 2, 1, 3).reshape(N_DP * HEADS, SEQ_LEN, HEAD_DIM)

    def to_tokens(array):
        return array.reshape(N_DP, HEADS, SEQ_LEN, HEAD_DIM).transpose(0, 2, 1, 3).reshape(TOKENS, width)

    seq_index = (jnp.arange(N_DP * HEADS) // HEADS).astype(jnp.int32)
    sec_table = section_ids.reshape(N_DP, SEQ_LEN)
    flag_table = masked.reshape(N_DP, SEQ_LEN)

    def per_item(packed):
        query_h, key_h, value_h, grad_h, which = packed
        return head_backward(query_h, key_h, value_h, grad_h, sec_table[which], flag_table[which])

    results = lax.map(per_item, (to_heads(queries), to_heads(keys), to_heads(values), to_heads(attn_grad), seq_index))
    attn_out = to_tokens(results[0])
    query_grad = to_tokens(results[1])
    key_grad = to_tokens(results[2])
    value_grad = to_tokens(results[3])
    weight_grad = jnp.dot(attn_out.T, out_grad, preferred_element_type=jnp.float32)
    return query_grad, key_grad, value_grad, weight_grad
```

```python
import jax
import jax.numpy as jnp
from jax import lax
from jax.sharding import PartitionSpec as P

HEAD_DIM = 128


def local(queries, keys, values, out_grad, out_weight, section_ids, masked):
    score_scale = HEAD_DIM ** (-0.5)
    attn_grad = lax.dot_general(
        out_grad,
        lax.all_gather(out_weight, "dp", axis=0, tiled=True),
        (((1,), (1,)), ((), ())),
        preferred_element_type=jnp.float32,
    ).astype(jnp.bfloat16)
    query_h, key_h, value_h = (
        lax.all_to_all(queries, "seq", split_axis=1, concat_axis=0, tiled=True),
        lax.all_to_all(keys, "seq", split_axis=1, concat_axis=0, tiled=True),
        lax.all_to_all(values, "seq", split_axis=1, concat_axis=0, tiled=True),
    )
    grad_h = lax.all_to_all(attn_grad, "seq", split_axis=1, concat_axis=0, tiled=True)
    n_seq = lax.axis_size("seq")
    code = section_ids * 2 + masked
    code_all = lax.all_to_all(
        jnp.broadcast_to(code[None], (n_seq,) + code.shape), "seq", 0, 0, tiled=True
    ).reshape(-1)
    sec_all = code_all // 2
    flag_all = code_all - 2 * sec_all
    grad_plane = lax.all_gather(out_grad, "dp", axis=0, tiled=True)
    seq_span = query_h.shape[0]
    width_here = query_h.shape[1]
    heads_here = width_here // HEAD_DIM
    block_rows = min(512, seq_span)
    num_blocks = seq_span // block_rows
    keys_head = key_h.reshape(seq_span, heads_here, HEAD_DIM)
    values_head = value_h.reshape(seq_span, heads_here, HEAD_DIM)
    visible_key = flag_all == 0

    def block_step(carried, block_item):
        key_acc, value_acc = carried
        query_blk, grad_blk, sec_blk = block_item
        scores = (
            jnp.einsum("qhd,khd->hqk", query_blk, keys_head, preferred_element_type=jnp.float32)
            * score_scale
        )
        allowed = visible_key[None, :] | (sec_blk[:, None] == sec_all[None, :])
        scores = jnp.where(allowed[None], scores, -1e30)
        row_max = jnp.max(scores, axis=2, keepdims=True)
        exp_scores = jnp.exp(scores - row_max)
        attn_probs = exp_scores / jnp.sum(exp_scores, axis=2, keepdims=True)
        probs_low = attn_probs.astype(jnp.bfloat16)
        out_blk = jnp.einsum(
            "hqk,khd->qhd", probs_low, values_head, preferred_element_type=jnp.float32
        ).astype(jnp.bfloat16)
        row_delta = jnp.sum(grad_blk.astype(jnp.float32) * out_blk.astype(jnp.float32), axis=2)
        prob_grad = jnp.einsum(
            "qhd,khd->hqk", grad_blk, values_head, preferred_element_type=jnp.float32
        )
        score_grad = (attn_probs * (prob_grad - row_delta.T[:, :, None])).astype(jnp.bfloat16)
        query_blk_grad = (
            jnp.einsum("hqk,khd->qhd", score_grad, keys_head, preferred_element_type=jnp.float32)
            * score_scale
        ).astype(jnp.bfloat16)
        key_acc = key_acc + jnp.einsum(
            "hqk,qhd->khd", score_grad, query_blk, preferred_element_type=jnp.float32
        )
        value_acc = value_acc + jnp.einsum(
            "hqk,qhd->khd", probs_low, grad_blk, preferred_element_type=jnp.float32
        )
        return ((key_acc, value_acc), (out_blk, query_blk_grad))

    scan_inputs = (
        query_h.reshape(num_blocks, block_rows, heads_here, HEAD_DIM),
        grad_h.reshape(num_blocks, block_rows, heads_here, HEAD_DIM),
        sec_all.reshape(num_blocks, block_rows),
    )
    zero_acc = jnp.zeros((seq_span, heads_here, HEAD_DIM), jnp.float32)
    (key_acc, value_acc), (out_blocks, query_blocks) = lax.scan(
        block_step, (zero_acc, zero_acc), scan_inputs
    )
    out_head = out_blocks.reshape(seq_span, width_here)
    query_grad_h = query_blocks.reshape(seq_span, width_here)
    key_grad_h = (key_acc * score_scale).astype(jnp.bfloat16).reshape(seq_span, width_here)
    value_grad_h = value_acc.astype(jnp.bfloat16).reshape(seq_span, width_here)
    attn_out, query_grad, key_grad, value_grad = (
        lax.all_to_all(out_head, "seq", split_axis=0, concat_axis=1, tiled=True),
        lax.all_to_all(query_grad_h, "seq", split_axis=0, concat_axis=1, tiled=True),
        lax.all_to_all(key_grad_h, "seq", split_axis=0, concat_axis=1, tiled=True),
        lax.all_to_all(value_grad_h, "seq", split_axis=0, concat_axis=1, tiled=True),
    )
    out_plane = lax.all_to_all(attn_out, "dp", split_axis=1, concat_axis=0, tiled=True)
    weight_grad = lax.psum(
        lax.dot_general(
            out_plane, grad_plane, (((0,), (0,)), ((), ())), preferred_element_type=jnp.float32
        ),
        "seq",
    )
    return (query_grad, key_grad, value_grad, weight_grad)


def solution(mesh):
    placed = (
        P(("dp", "seq"), None),
        P(("dp", "seq"), None),
        P(("dp", "seq"), None),
        P(("dp", "seq"), None),
        P("dp", None),
        P(("dp", "seq")),
        P(("dp", "seq")),
    )
    return jax.shard_map(
        local,
        mesh=mesh,
        in_specs=placed,
        out_specs=(
            P(("dp", "seq"), None),
            P(("dp", "seq"), None),
            P(("dp", "seq"), None),
            P("dp", None),
        ),
        check_vma=False,
    )
```
